32 devices in a mesh: gx: 4 (over y, x), gy: 8 (over z, core).
Axes of the slice: x: 2, y: 2, z: 4, core: 2. Of those that a mesh axis runs over, the one named last changes fastest.
Arguments:
- box_weights: float32 [512, 1024, 128], P('gx', 'gy'), may hold values from -6 to 6
- slowness: float32 [512, 1024], P('gx', 'gy'), may hold values from 0.5 to 2
- interpolation: float32 [4, 2, 2, 64, 64], replicated, may hold values from -0.5 to 0.5
- phase_rates: float32 [4, 3, 64], replicated, may hold values from -3 to 3
Outputs:
- level_weights: float32 [512, 1024, 128], P('gx', 'gy')
The draws below stay inside these ranges and needn't reach their ends.
All inputs are finite; a program needn't handle non-finite values.
Results may differ from the reference program's by a relative error of at most 0.0003.
Values sent between devices are 32-bit elements; how exact they have to be, the bound alone decides.
No kernel may reach another device: no remote copies, remote signals or barrier semaphores. Data moves between devices by JAX's collectives and lax.ppermute only.
A program may use at most 128 MiB of HBM per device.

```python
import jax
import jax.numpy as jnp
from jax import lax

R = 64
LEVELS = 4
CX = 128
CY = 128
BXX = 512
BYY = 1024
N_GX = 4
N_GY = 8


def level_of(own_key, shape, shards, least, largest):
    level, own = 1.0, jax.random.fold_in(own_key, 6)
    for axis_at, parts in shards:
        steps = jnp.exp(jax.random.uniform(jax.random.fold_in(own, axis_at), (parts,), jnp.float32, least / len(shards), largest / len(shards)))
        level = level * jnp.repeat(steps, shape[axis_at] // parts).reshape([-1 if axis == axis_at else 1 for axis in range(len(shape))])
    return level


def gaussian(stream_key, shape, scale, limit, shards=(), held_as=jnp.bfloat16):
    gain = level_of(stream_key, shape, shards, -0.22, 0.18) if shards else 1.0
    values = jax.random.normal(stream_key, shape, jnp.float32) * scale * gain
    return jnp.minimum(jnp.maximum(values, -limit), limit).astype(held_as)


def setup_inputs(seed: int = 0) -> dict:
    key_list = jax.random.split(jax.random.key(seed), 5)
    return {
        "box_weights": gaussian(key_list[0], (BXX, BYY, 2 * R), 1.0, 6.0, ((0, 4), (1, 8)), jnp.float32),
        "slowness": jnp.clip(0.5 + 1.5 * jax.random.uniform(key_list[1], (BXX, BYY), jnp.float32) ** level_of(key_list[1], (BXX, BYY), ((0, 4), (1, 8)), -0.2, 0.2), 0.5, 2.0),
        "interpolation": gaussian(key_list[2], (LEVELS, 2, 2, R, R), (2 * R) ** -0.5, 0.5, (), jnp.float32),
        "phase_rates": jnp.clip(jax.random.uniform(key_list[3], (LEVELS, 3, R), jnp.float32, -3.0, 3.0), -3.0, 3.0),
    }


HIGH = lax.Precision.HIGHEST


def interp_matrix(interpolation, level_index, upper):
    self_part = interpolation[level_index, upper, 0]
    peer_part = interpolation[level_index, upper, 1]
    zeros_block = jnp.zeros_like(self_part)
    return jnp.concatenate([
        jnp.concatenate([self_part, zeros_block], 1),
        jnp.concatenate([zeros_block, self_part], 1),
        jnp.concatenate([peer_part, zeros_block], 1),
        jnp.concatenate([zeros_block, peer_part], 1)], 0)


def combine(own_rows, partner, mixer):
    stacked = jnp.concatenate([own_rows, partner], -1)
    return jnp.matmul(stacked, mixer, precision=HIGH)


def rotate(combined, x_position, y_position, slowness_here, rates):
    angles = x_position[..., None] * rates[0] + y_position[..., None] * rates[1] + slowness_here[..., None] * rates[2]
    angles = jnp.concatenate([angles, angles], -1)
    half_width = combined.shape[-1] // 2
    turned = jnp.concatenate([-combined[..., half_width:], combined[..., :half_width]], -1)
    return jnp.cos(angles) * combined + jnp.sin(angles) * turned


def level_along_x(current, slowness, interpolation, phase_rates, level_index, level_bit):
    lower_mixer = interp_matrix(interpolation, level_index, 0)
    upper_mixer = interp_matrix(interpolation, level_index, 1)
    x_position = (jnp.arange(BXX, dtype=jnp.int32).astype(jnp.float32) + 0.5) / BXX
    run_length = (1 << level_bit) * CX
    run_count = BXX // (2 * run_length)

    def step(block_index, current):
        offset = (block_index * CY).astype(jnp.int32)
        piece = lax.dynamic_slice_in_dim(current, offset, CY, 1)
        slowness_here = lax.dynamic_slice_in_dim(slowness, offset, CY, 1)
        y_position = ((offset + jnp.arange(CY, dtype=jnp.int32)).astype(jnp.float32) + 0.5) / BYY
        grouped = piece.reshape(run_count, 2, run_length, CY, 2 * R)
        partner = grouped[:, ::-1]
        low_half = combine(grouped[:, 0], partner[:, 0], lower_mixer)
        high_half = combine(grouped[:, 1], partner[:, 1], upper_mixer)
        combined = jnp.stack([low_half, high_half], 1).reshape(BXX, CY, 2 * R)
        updated = rotate(combined, x_position[:, None], y_position[None, :], slowness_here, phase_rates[level_index])
        return lax.dynamic_update_slice_in_dim(current, updated, offset, 1)

    return lax.fori_loop(0, N_GY, step, current)


def level_along_y(current, slowness, interpolation, phase_rates, level_index, level_bit):
    lower_mixer = interp_matrix(interpolation, level_index, 0)
    upper_mixer = interp_matrix(interpolation, level_index, 1)
    y_position = (jnp.arange(BYY, dtype=jnp.int32).astype(jnp.float32) + 0.5) / BYY
    run_length = (1 << level_bit) * CY
    run_count = BYY // (2 * run_length)

    def step(block_index, current):
        offset = (block_index * CX).astype(jnp.int32)
        piece = lax.dynamic_slice_in_dim(current, offset, CX, 0)
        slowness_here = lax.dynamic_slice_in_dim(slowness, offset, CX, 0)
        x_position = ((offset + jnp.arange(CX, dtype=jnp.int32)).astype(jnp.float32) + 0.5) / BXX
        grouped = piece.reshape(CX, run_count, 2, run_length, 2 * R)
        partner = grouped[:, :, ::-1]
        low_half = combine(grouped[:, :, 0], partner[:, :, 0], lower_mixer)
        high_half = combine(grouped[:, :, 1], partner[:, :, 1], upper_mixer)
        combined = jnp.stack([low_half, high_half], 2).reshape(CX, BYY, 2 * R)
        updated = rotate(combined, x_position[:, None], y_position[None, :], slowness_here, phase_rates[level_index])
        return lax.dynamic_update_slice_in_dim(current, updated, offset, 0)

    return lax.fori_loop(0, N_GX, step, current)


def reference(box_weights, slowness, interpolation, phase_rates):
    current = box_weights
    for level_index in range(LEVELS):
        if level_index % 2 == 0:
            level_bit = N_GX.bit_length() - 2 - level_index // 2
            current = level_along_x(current, slowness, interpolation, phase_rates, level_index, level_bit)
        else:
            level_bit = N_GY.bit_length() - 2 - level_index // 2
            current = level_along_y(current, slowness, interpolation, phase_rates, level_index, level_bit)
    return current
```

```python
import jax
import jax.numpy as jnp
from jax import lax
from jax.sharding import PartitionSpec as P

LEVELS = 4
CHUNKS = 8


HIGH = lax.Precision.HIGHEST


def swapped(x, axis, distance):
    return lax.ppermute(x, axis, [(i, i ^ 1 << distance) for i in range(lax.axis_size(axis))])


def interp_matrix(interpolation, level_index, upper):
    self_part = interpolation[level_index, upper, 0]
    peer_part = interpolation[level_index, upper, 1]
    zeros_block = jnp.zeros_like(self_part)
    return jnp.concatenate(
        [
            jnp.concatenate([self_part, zeros_block], 1),
            jnp.concatenate([zeros_block, self_part], 1),
            jnp.concatenate([peer_part, zeros_block], 1),
            jnp.concatenate([zeros_block, peer_part], 1),
        ],
        0,
    )


def combine(own_rows, partner, mixer):
    stacked = jnp.concatenate([own_rows, partner], -1)
    return jnp.matmul(stacked, mixer, precision=HIGH)


def rotate(combined, x_position, y_position, slowness_here, rates):
    angles = (
        x_position[..., None] * rates[0]
        + y_position[..., None] * rates[1]
        + slowness_here[..., None] * rates[2]
    )
    angles = jnp.concatenate([angles, angles], -1)
    half_width = combined.shape[-1] // 2
    turned = jnp.concatenate([-combined[..., half_width:], combined[..., :half_width]], -1)
    return jnp.cos(angles) * combined + jnp.sin(angles) * turned


def per_device(box_weights, slowness, interpolation, phase_rates):
    count_x = lax.axis_size("gx")
    count_y = lax.axis_size("gy")
    rows_x, rows_y, channels = box_weights.shape
    total_x = rows_x * count_x
    total_y = rows_y * count_y
    index_x = lax.axis_index("gx") * rows_x + jnp.arange(rows_x, dtype=jnp.int32)
    index_y = lax.axis_index("gy") * rows_y + jnp.arange(rows_y, dtype=jnp.int32)
    x_position = (index_x.astype(jnp.float32) + 0.5) / total_x
    y_position = (index_y.astype(jnp.float32) + 0.5) / total_y

    mixers = []
    for level_index in range(LEVELS):
        lower_mixer = interp_matrix(interpolation, level_index, 0)
        upper_mixer = interp_matrix(interpolation, level_index, 1)
        if level_index % 2 == 0:
            level_bit = count_x.bit_length() - 2 - level_index // 2
            axis = "gx"
        else:
            level_bit = count_y.bit_length() - 2 - level_index // 2
            axis = "gy"
        upper_side = lax.axis_index(axis) >> level_bit & 1
        mixers.append((axis, level_bit, jnp.where(upper_side == 1, upper_mixer, lower_mixer)))

    chunks = CHUNKS if rows_x % CHUNKS == 0 else 1
    step = rows_x // chunks
    state = [box_weights[c * step:(c + 1) * step] for c in range(chunks)]
    for wave in range(chunks + LEVELS - 1):
        for c in range(chunks):
            level_index = wave - c
            if not 0 <= level_index < LEVELS:
                continue
            axis, level_bit, mixer = mixers[level_index]
            current = state[c]
            partner = swapped(current, axis, level_bit)
            combined = combine(current, partner, mixer)
            state[c] = rotate(
                combined,
                x_position[c * step:(c + 1) * step, None],
                y_position[None, :],
                slowness[c * step:(c + 1) * step],
                phase_rates[level_index],
            )
    return jnp.concatenate(state, 0)


def solution(mesh):
    in_specs = (P("gx", "gy", None), P("gx", "gy"), P(), P())
    out_specs = P("gx", "gy", None)
    return jax.shard_map(
        per_device, mesh=mesh, in_specs=in_specs, out_specs=out_specs, check_vma=False
    )
```

```python
import jax
import jax.numpy as jnp
from jax import lax
from jax.sharding import PartitionSpec as P

LEVELS = 4
CHUNKS = 8
TIE_LAG = 1
FINAL_LAG = 2


HIGH = lax.Precision.HIGHEST


def swapped(x, axis, distance):
    return lax.ppermute(x, axis, [(i, i ^ 1 << distance) for i in range(lax.axis_size(axis))])


def interp_matrix(interpolation, level_index, upper):
    self_part = interpolation[level_index, upper, 0]
    peer_part = interpolation[level_index, upper, 1]
    zeros_block = jnp.zeros_like(self_part)
    return jnp.concatenate(
        [
            jnp.concatenate([self_part, zeros_block], 1),
            jnp.concatenate([zeros_block, self_part], 1),
            jnp.concatenate([peer_part, zeros_block], 1),
            jnp.concatenate([zeros_block, peer_part], 1),
        ],
        0,
    )


def combine(own_rows, partner, mixer):
    stacked = jnp.concatenate([own_rows, partner], -1)
    return jnp.matmul(stacked, mixer, precision=HIGH)


def rotate(combined, x_position, y_position, slowness_here, rates):
    angles = (
        x_position[..., None] * rates[0]
        + y_position[..., None] * rates[1]
        + slowness_here[..., None] * rates[2]
    )
    angles = jnp.concatenate([angles, angles], -1)
    half_width = combined.shape[-1] // 2
    turned = jnp.concatenate([-combined[..., half_width:], combined[..., :half_width]], -1)
    return jnp.cos(angles) * combined + jnp.sin(angles) * turned


def per_device(box_weights, slowness, interpolation, phase_rates):
    count_x = lax.axis_size("gx")
    count_y = lax.axis_size("gy")
    rows_x, rows_y, channels = box_weights.shape
    total_x = rows_x * count_x
    total_y = rows_y * count_y
    index_x = lax.axis_index("gx") * rows_x + jnp.arange(rows_x, dtype=jnp.int32)
    index_y = lax.axis_index("gy") * rows_y + jnp.arange(rows_y, dtype=jnp.int32)
    x_position = (index_x.astype(jnp.float32) + 0.5) / total_x
    y_position = (index_y.astype(jnp.float32) + 0.5) / total_y

    mixers = []
    for level_index in range(LEVELS):
        lower_mixer = interp_matrix(interpolation, level_index, 0)
        upper_mixer = interp_matrix(interpolation, level_index, 1)
        if level_index % 2 == 0:
            level_bit = count_x.bit_length() - 2 - level_index // 2
            axis = "gx"
        else:
            level_bit = count_y.bit_length() - 2 - level_index // 2
            axis = "gy"
        upper_side = lax.axis_index(axis) >> level_bit & 1
        mixers.append((axis, level_bit, jnp.where(upper_side == 1, upper_mixer, lower_mixer)))

    chunks = CHUNKS if rows_x % CHUNKS == 0 else 1
    step = rows_x // chunks

    value = {(c, 0): box_weights[c * step:(c + 1) * step] for c in range(chunks)}
    sent = {}

    group_of = {}
    for s in range(chunks + max(TIE_LAG, FINAL_LAG)):
        members = [(s, 2), (s - TIE_LAG, 3), (s - FINAL_LAG, LEVELS)]
        members = [m for m in members if 0 <= m[0] < chunks]
        if len(members) > 1:
            for m in members:
                group_of[m] = members

    def raw(c, l):
        if (c, l) not in value:
            prev = held(c, l - 1)
            if (c, l - 1) not in sent:
                axis, level_bit, _ = mixers[l - 1]
                sent[(c, l - 1)] = swapped(prev, axis, level_bit)
            _, _, mixer = mixers[l - 1]
            combined = combine(prev, sent[(c, l - 1)], mixer)
            value[(c, l)] = rotate(
                combined,
                x_position[c * step:(c + 1) * step, None],
                y_position[None, :],
                slowness[c * step:(c + 1) * step],
                phase_rates[l - 1],
            )
        return value[(c, l)]

    tied = {}

    def held(c, l):
        if (c, l) in tied:
            return tied[(c, l)]
        if (c, l) not in group_of:
            return raw(c, l)
        members = group_of[(c, l)]
        outs = lax.optimization_barrier(tuple(raw(*m) for m in members))
        for m, o in zip(members, outs):
            tied[m] = o
        return tied[(c, l)]

    for c in range(chunks):
        axis, level_bit, _ = mixers[0]
        sent[(c, 0)] = swapped(value[(c, 0)], axis, level_bit)
    for c in range(chunks):
        raw(c, 2)
    results = [held(c, LEVELS) for c in range(chunks)]
    return jnp.concatenate(results, 0)


def solution(mesh):
    in_specs = (P("gx", "gy", None), P("gx", "gy"), P(), P())
    out_specs = P("gx", "gy", None)
    return jax.shard_map(
        per_device, mesh=mesh, in_specs=in_specs, out_specs=out_specs, check_vma=False
    )
```

```python
import jax
import jax.numpy as jnp
from jax import lax
from jax.sharding import PartitionSpec as P

LEVELS = 4
CHUNKS = 8
GROUP = ((1, 0), (2, 4), (3, 5), (LEVELS, 7))


HIGH = lax.Precision.HIGHEST


def swapped(x, axis, distance):
    return lax.ppermute(x, axis, [(i, i ^ 1 << distance) for i in range(lax.axis_size(axis))])


def interp_matrix(interpolation, level_index, upper):
    self_part = interpolation[level_index, upper, 0]
    peer_part = interpolation[level_index, upper, 1]
    zeros_block = jnp.zeros_like(self_part)
    return jnp.concatenate(
        [
            jnp.concatenate([self_part, zeros_block], 1),
            jnp.concatenate([zeros_block, self_part], 1),
            jnp.concatenate([peer_part, zeros_block], 1),
            jnp.concatenate([zeros_block, peer_part], 1),
        ],
        0,
    )


def combine(own_rows, partner, mixer):
    stacked = jnp.concatenate([own_rows, partner], -1)
    return jnp.matmul(stacked, mixer, precision=HIGH)


def rotate(combined, x_position, y_position, slowness_here, rates):
    angles = (
        x_position[..., None] * rates[0]
        + y_position[..., None] * rates[1]
        + slowness_here[..., None] * rates[2]
    )
    angles = jnp.concatenate([angles, angles], -1)
    half_width = combined.shape[-1] // 2
    turned = jnp.concatenate([-combined[..., half_width:], combined[..., :half_width]], -1)
    return jnp.cos(angles) * combined + jnp.sin(angles) * turned


def per_device(box_weights, slowness, interpolation, phase_rates):
    count_x = lax.axis_size("gx")
    count_y = lax.axis_size("gy")
    rows_x, rows_y, channels = box_weights.shape
    total_x = rows_x * count_x
    total_y = rows_y * count_y
    index_x = lax.axis_index("gx") * rows_x + jnp.arange(rows_x, dtype=jnp.int32)
    index_y = lax.axis_index("gy") * rows_y + jnp.arange(rows_y, dtype=jnp.int32)
    x_position = (index_x.astype(jnp.float32) + 0.5) / total_x
    y_position = (index_y.astype(jnp.float32) + 0.5) / total_y

    mixers = []
    for level_index in range(LEVELS):
        lower_mixer = interp_matrix(interpolation, level_index, 0)
        upper_mixer = interp_matrix(interpolation, level_index, 1)
        if level_index % 2 == 0:
            level_bit = count_x.bit_length() - 2 - level_index // 2
            axis = "gx"
        else:
            level_bit = count_y.bit_length() - 2 - level_index // 2
            axis = "gy"
        upper_side = lax.axis_index(axis) >> level_bit & 1
        mixers.append((axis, level_bit, jnp.where(upper_side == 1, upper_mixer, lower_mixer)))

    chunks = CHUNKS if rows_x % CHUNKS == 0 else 1
    step = rows_x // chunks

    value = {(c, 0): box_weights[c * step:(c + 1) * step] for c in range(chunks)}
    sent = {}

    group_of = {}
    for s in range(chunks + max(lag for _, lag in GROUP)):
        members = [(s - lag, level) for level, lag in GROUP]
        members = [m for m in members if 0 <= m[0] < chunks]
        if len(members) > 1:
            for m in members:
                group_of[m] = members

    def raw(c, l):
        if (c, l) not in value:
            prev = held(c, l - 1)
            if (c, l - 1) not in sent:
                axis, level_bit, _ = mixers[l - 1]
                sent[(c, l - 1)] = swapped(prev, axis, level_bit)
            _, _, mixer = mixers[l - 1]
            combined = combine(prev, sent[(c, l - 1)], mixer)
            value[(c, l)] = rotate(
                combined,
                x_position[c * step:(c + 1) * step, None],
                y_position[None, :],
                slowness[c * step:(c + 1) * step],
                phase_rates[l - 1],
            )
        return value[(c, l)]

    tied = {}

    def held(c, l):
        if (c, l) in tied:
            return tied[(c, l)]
        if (c, l) not in group_of:
            return raw(c, l)
        members = group_of[(c, l)]
        outs = lax.optimization_barrier(tuple(raw(*m) for m in members))
        for m, o in zip(members, outs):
            tied[m] = o
        return tied[(c, l)]

    for c in range(chunks):
        axis, level_bit, _ = mixers[0]
        sent[(c, 0)] = swapped(value[(c, 0)], axis, level_bit)
    results = [held(c, LEVELS) for c in range(chunks)]
    return jnp.concatenate(results, 0)


def solution(mesh):
    in_specs = (P("gx", "gy", None), P("gx", "gy"), P(), P())
    out_specs = P("gx", "gy", None)
    return jax.shard_map(
        per_device, mesh=mesh, in_specs=in_specs, out_specs=out_specs, check_vma=False
    )
```

```python
import jax
import jax.numpy as jnp
from jax import lax
from jax.sharding import PartitionSpec as P

LEVELS = 4
CHUNKS = 8
GROUP = ((1, 0), (2, 4), (3, 5), (LEVELS, 7))


HIGH = lax.Precision.HIGHEST


def swapped(x, axis, distance):
    return lax.ppermute(x, axis, [(i, i ^ 1 << distance) for i in range(lax.axis_size(axis))])


def interp_matrix(interpolation, level_index, upper):
    self_part = interpolation[level_index, upper, 0]
    peer_part = interpolation[level_index, upper, 1]
    zeros_block = jnp.zeros_like(self_part)
    return jnp.concatenate(
        [
            jnp.concatenate([self_part, zeros_block], 1),
            jnp.concatenate([zeros_block, self_part], 1),
            jnp.concatenate([peer_part, zeros_block], 1),
            jnp.concatenate([zeros_block, peer_part], 1),
        ],
        0,
    )


def combine(own_rows, partner, mixer):
    stacked = jnp.concatenate([own_rows, partner], -1)
    return jnp.matmul(stacked, mixer, precision=HIGH)


def rotate(combined, x_position, y_position, slowness_here, rates):
    angles = (
        x_position[..., None] * rates[0]
        + y_position[..., None] * rates[1]
        + slowness_here[..., None] * rates[2]
    )
    angles = jnp.concatenate([angles, angles], -1)
    half_width = combined.shape[-1] // 2
    turned = jnp.concatenate([-combined[..., half_width:], combined[..., :half_width]], -1)
    return jnp.cos(angles) * combined + jnp.sin(angles) * turned


def per_device(box_weights, slowness, interpolation, phase_rates):
    count_x = lax.axis_size("gx")
    count_y = lax.axis_size("gy")
    rows_x, rows_y, channels = box_weights.shape
    total_x = rows_x * count_x
    total_y = rows_y * count_y
    index_x = lax.axis_index("gx") * rows_x + jnp.arange(rows_x, dtype=jnp.int32)
    index_y = lax.axis_index("gy") * rows_y + jnp.arange(rows_y, dtype=jnp.int32)
    x_position = (index_x.astype(jnp.float32) + 0.5) / total_x
    y_position = (index_y.astype(jnp.float32) + 0.5) / total_y

    mixers = []
    for level_index in range(LEVELS):
        lower_mixer = interp_matrix(interpolation, level_index, 0)
        upper_mixer = interp_matrix(interpolation, level_index, 1)
        if level_index % 2 == 0:
            level_bit = count_x.bit_length() - 2 - level_index // 2
            axis = "gx"
        else:
            level_bit = count_y.bit_length() - 2 - level_index // 2
            axis = "gy"
        upper_side = lax.axis_index(axis) >> level_bit & 1
        mixers.append((axis, level_bit, jnp.where(upper_side == 1, upper_mixer, lower_mixer)))

    chunks = CHUNKS if rows_x % CHUNKS == 0 else 1
    step = rows_x // chunks

    value = {(c, 0): box_weights[c * step:(c + 1) * step] for c in range(chunks)}
    sent = {}

    group_of = {}
    groups = []
    for s in range(chunks + max(lag for _, lag in GROUP)):
        members = [(s - lag, level) for level, lag in GROUP]
        members = [m for m in members if 0 <= m[0] < chunks]
        if len(members) > 1:
            for m in members:
                group_of[m] = len(groups)
            groups.append(members)

    def raw(c, l):
        if (c, l) not in value:
            prev = held(c, l - 1)
            if (c, l - 1) not in sent:
                axis, level_bit, _ = mixers[l - 1]
                sent[(c, l - 1)] = swapped(prev, axis, level_bit)
            _, _, mixer = mixers[l - 1]
            combined = combine(prev, sent[(c, l - 1)], mixer)
            value[(c, l)] = rotate(
                combined,
                x_position[c * step:(c + 1) * step, None],
                y_position[None, :],
                slowness[c * step:(c + 1) * step],
                phase_rates[l - 1],
            )
        return value[(c, l)]

    tied = {}

    def held(c, l):
        if (c, l) in tied:
            return tied[(c, l)]
        if (c, l) not in group_of:
            return raw(c, l)
        index = group_of[(c, l)]
        members = groups[index]
        before = tuple(held(*m) for m in groups[index - 1]) if index > 0 else ()
        outs, _ = lax.optimization_barrier((tuple(raw(*m) for m in members), before))
        for m, o in zip(members, outs):
            tied[m] = o
        return tied[(c, l)]

    for c in range(chunks):
        axis, level_bit, _ = mixers[0]
        sent[(c, 0)] = swapped(value[(c, 0)], axis, level_bit)
    results = [held(c, LEVELS) for c in range(chunks)]
    return jnp.concatenate(results, 0)


def solution(mesh):
    in_specs = (P("gx", "gy", None), P("gx", "gy"), P(), P())
    out_specs = P("gx", "gy", None)
    return jax.shard_map(
        per_device, mesh=mesh, in_specs=in_specs, out_specs=out_specs, check_vma=False
    )
```

```python
import jax
import jax.numpy as jnp
from jax import lax
from jax.sharding import PartitionSpec as P

LEVELS = 4
CHUNKS = 8
GROUP = ((1, 0), (2, 4), (3, 5), (LEVELS, 6))


HIGH = lax.Precision.HIGHEST


def swapped(x, axis, distance):
    return lax.ppermute(x, axis, [(i, i ^ 1 << distance) for i in range(lax.axis_size(axis))])


def interp_matrix(interpolation, level_index, upper):
    self_part = interpolation[level_index, upper, 0]
    peer_part = interpolation[level_index, upper, 1]
    zeros_block = jnp.zeros_like(self_part)
    return jnp.concatenate(
        [
            jnp.concatenate([self_part, zeros_block], 1),
            jnp.concatenate([zeros_block, self_part], 1),
            jnp.concatenate([peer_part, zeros_block], 1),
            jnp.concatenate([zeros_block, peer_part], 1),
        ],
        0,
    )


def combine(own_rows, partner, mixer):
    stacked = jnp.concatenate([own_rows, partner], -1)
    return jnp.matmul(stacked, mixer, precision=HIGH)


def rotate(combined, x_position, y_position, slowness_here, rates):
    angles = (
        x_position[..., None] * rates[0]
        + y_position[..., None] * rates[1]
        + slowness_here[..., None] * rates[2]
    )
    angles = jnp.concatenate([angles, angles], -1)
    half_width = combined.shape[-1] // 2
    turned = jnp.concatenate([-combined[..., half_width:], combined[..., :half_width]], -1)
    return jnp.cos(angles) * combined + jnp.sin(angles) * turned


def per_device(box_weights, slowness, interpolation, phase_rates):
    count_x = lax.axis_size("gx")
    count_y = lax.axis_size("gy")
    rows_x, rows_y, channels = box_weights.shape
    total_x = rows_x * count_x
    total_y = rows_y * count_y
    index_x = lax.axis_index("gx") * rows_x + jnp.arange(rows_x, dtype=jnp.int32)
    index_y = lax.axis_index("gy") * rows_y + jnp.arange(rows_y, dtype=jnp.int32)
    x_position = (index_x.astype(jnp.float32) + 0.5) / total_x
    y_position = (index_y.astype(jnp.float32) + 0.5) / total_y

    mixers = []
    for level_index in range(LEVELS):
        lower_mixer = interp_matrix(interpolation, level_index, 0)
        upper_mixer = interp_matrix(interpolation, level_index, 1)
        if level_index % 2 == 0:
            level_bit = count_x.bit_length() - 2 - level_index // 2
            axis = "gx"
        else:
            level_bit = count_y.bit_length() - 2 - level_index // 2
            axis = "gy"
        upper_side = lax.axis_index(axis) >> level_bit & 1
        mixers.append((axis, level_bit, jnp.where(upper_side == 1, upper_mixer, lower_mixer)))

    chunks = CHUNKS if rows_x % CHUNKS == 0 else 1
    step = rows_x // chunks

    value = {(c, 0): box_weights[c * step:(c + 1) * step] for c in range(chunks)}
    sent = {}

    group_of = {}
    groups = []
    for s in range(chunks + max(lag for _, lag in GROUP)):
        members = [(s - lag, level) for level, lag in GROUP]
        members = [m for m in members if 0 <= m[0] < chunks]
        if len(members) > 1:
            for m in members:
                group_of[m] = len(groups)
            groups.append(members)

    def raw(c, l):
        if (c, l) not in value:
            prev = held(c, l - 1)
            if (c, l - 1) not in sent:
                axis, level_bit, _ = mixers[l - 1]
                sent[(c, l - 1)] = swapped(prev, axis, level_bit)
            _, _, mixer = mixers[l - 1]
            combined = combine(prev, sent[(c, l - 1)], mixer)
            value[(c, l)] = rotate(
                combined,
                x_position[c * step:(c + 1) * step, None],
                y_position[None, :],
                slowness[c * step:(c + 1) * step],
                phase_rates[l - 1],
            )
        return value[(c, l)]

    tied = {}

    def held(c, l):
        if (c, l) in tied:
            return tied[(c, l)]
        if (c, l) not in group_of:
            return raw(c, l)
        index = group_of[(c, l)]
        members = groups[index]
        before = tuple(held(*m) for m in groups[index - 1]) if index > 0 else ()
        outs, _ = lax.optimization_barrier((tuple(raw(*m) for m in members), before))
        for m, o in zip(members, outs):
            tied[m] = o
        return tied[(c, l)]

    for c in range(chunks):
        axis, level_bit, _ = mixers[0]
        sent[(c, 0)] = swapped(value[(c, 0)], axis, level_bit)
    results = [held(c, LEVELS) for c in range(chunks)]
    return jnp.concatenate(results, 0)


def solution(mesh):
    in_specs = (P("gx", "gy", None), P("gx", "gy"), P(), P())
    out_specs = P("gx", "gy", None)
    return jax.shard_map(
        per_device, mesh=mesh, in_specs=in_specs, out_specs=out_specs, check_vma=False
    )
```
